1024 devices in a mesh: stretch: 16 (over y_hi, x, core), ctx: 64 (over y_lo, z).
Axes of the slice: x: 4, y: 8 (y_hi: 2, y_lo: 4; y = y_hi * 4 + y_lo), z: 16, core: 2. Of those that a mesh axis runs over, the one named last changes fastest.
Arguments:
- hidden_in: bfloat16 [131072, 5120], P(('stretch', 'ctx')), may hold values from -6 to 6
- query_weight: bfloat16 [5120, 384], P('ctx', 'stretch'), may hold values from -0.078125 to 0.078125
- stored_keys: bfloat16 [131072, 128], P(('stretch', 'ctx')), may hold values from -6 to 6
- stored_values: bfloat16 [131072, 128], P(('stretch', 'ctx')), may hold values from -6 to 6
- kv_scale: bfloat16 [131072, 2], P(('stretch', 'ctx')), may hold values from 0.25 to 64
- doc_start: int32 [131072], P(('stretch', 'ctx')), may hold values from 0 to 8191, as said below
Outputs:
- attended: bfloat16 [131072, 384], P(('stretch', 'ctx'))
The draws below stay inside these ranges and needn't reach their ends.
Inputs may be any that keep to these rules, and one draw needn't show every extreme that they name: doc_start of a token is at most the token's own index inside its window, equals it at the first token of a document, is 0 at a window's first token and stays constant through a document; the last token of the first window is a document of its own.
All inputs are finite; a program needn't handle non-finite values.
Results may differ from the reference program's by a relative error of at most 0.0085.
The reference program's roundings to bfloat16 on the way (of `queries`, `keys`, `values` and `weights`) count: a program that leaves them out, or rounds other values in their place, can miss the bound.
Values may be sent and summed in bfloat16 or wider, within the bound.
No kernel may reach another device: no remote copies, remote signals or barrier semaphores. Data moves between devices by JAX's collectives and lax.ppermute only.
A program may use at most 32 MiB of HBM per device.

```python
import math
import jax
import jax.numpy as jnp
from jax import lax

D = 5120
HEAD_DIM = 128
QUERY_HEADS = 3
WINDOW = 8192
SEQUENCE_LENGTH = 131072


def draw_kv_scale(key, part):
    first = jax.random.fold_in(key, 0)
    output_lines = jnp.exp(jax.random.uniform(first, (SEQUENCE_LENGTH, 2), jnp.float32, math.log(0.5), math.log(2.0)))
    return output_lines.astype(jnp.bfloat16)


def draw_doc_start(key, part):
    flags = jax.random.randint(key, (SEQUENCE_LENGTH // WINDOW, WINDOW), 0, WINDOW) < 4
    index = jnp.arange(WINDOW, dtype=jnp.int32)[None, :]
    window_number = jnp.arange(SEQUENCE_LENGTH // WINDOW, dtype=jnp.int32)[:, None]
    flags = flags | (index == 0) | (index == WINDOW - 1) & (window_number == 0)
    starts = jnp.where(flags, index, 0).astype(jnp.int32)
    return lax.cummax(starts, axis=1).reshape(SEQUENCE_LENGTH).astype(jnp.int32)


def level_of(stream_key, dims, cuts, smallest, largest):
    def one(axis_at, parts):
        heights = jax.random.uniform(jax.random.fold_in(jax.random.fold_in(stream_key, 6), axis_at), (parts,), jnp.float32, smallest / len(cuts), largest / len(cuts))
        return jnp.repeat(jnp.exp(heights), dims[axis_at] // parts).reshape((-1,) + (1,) * (len(dims) - axis_at - 1))

    factor_of = one(*cuts[0])
    for cut in cuts[1:]:
        factor_of = factor_of * one(*cut)
    return factor_of


def scatter_about(rng, shape, spread, reach, cuts=(), kind=jnp.bfloat16):
    result = jax.random.normal(rng, shape, jnp.float32) * spread
    if len(cuts) > 0:
        result = level_of(rng, shape, cuts, -0.22, 0.18) * result
    return jnp.clip(result, min=-reach, max=reach).astype(kind)


def setup_inputs(seed: int = 0) -> dict:
    seeds = jax.random.split(jax.random.key(seed), 7)
    hidden_in = scatter_about(seeds[0], (SEQUENCE_LENGTH, D), 1.0, 6.0, ((0, 1024),))
    query_weight = scatter_about(seeds[1], (D, QUERY_HEADS * HEAD_DIM), D ** -0.5, 0.078125, ((0, 64), (1, 16)))
    stored_keys = scatter_about(seeds[2], (SEQUENCE_LENGTH, HEAD_DIM), 1.0, 6.0, ((0, 1024),))
    stored_values = scatter_about(seeds[3], (SEQUENCE_LENGTH, HEAD_DIM), 1.0, 6.0, ((0, 1024),))
    kv_scale = draw_kv_scale(jax.random.fold_in(seeds[6], 71), 0)
    doc_start = draw_doc_start(jax.random.fold_in(seeds[6], 71), 0)
    return dict(hidden_in=hidden_in, query_weight=query_weight, stored_keys=stored_keys, stored_values=stored_values, kv_scale=kv_scale, doc_start=doc_start)


def attend_group(q_group, k_group, v_group, start_group):
    block = math.gcd(WINDOW, 512)
    count = WINDOW // block
    q_blocks = q_group.reshape(count, block, QUERY_HEADS, HEAD_DIM)
    s_blocks = start_group.reshape(count, block)
    p_blocks = jnp.arange(WINDOW, dtype=jnp.int32).reshape(count, block)
    columns = jnp.arange(WINDOW, dtype=jnp.int32)

    def one_block(pieces):
        q_block, s_block, p_block = pieces
        scores = jnp.einsum('qhd,kd->hqk', q_block.astype(jnp.float32), k_group.astype(jnp.float32))
        allowed = (columns[None, :] >= s_block[:, None]) & (columns[None, :] <= p_block[:, None])
        scores = jnp.where(allowed[None], scores, -1e30)
        top = jnp.max(scores, axis=2, keepdims=True)
        weights = jnp.where(allowed[None], jnp.exp(scores - top), 0.0)
        total = jnp.sum(weights, axis=2)
        rounded = lax.optimization_barrier(weights.astype(jnp.bfloat16))
        mixed = jnp.einsum('hqk,kd->hqd', rounded.astype(jnp.float32), v_group.astype(jnp.float32))
        mixed = mixed / total[..., None]
        return jnp.transpose(mixed, (1, 0, 2)).astype(jnp.bfloat16)

    out = lax.map(one_block, (q_blocks, s_blocks, p_blocks))
    return out.reshape(WINDOW, QUERY_HEADS * HEAD_DIM)


def reference(hidden_in, query_weight, stored_keys, stored_values, kv_scale, doc_start):
    projected = jnp.dot(hidden_in, query_weight, preferred_element_type=jnp.float32)
    queries = (projected * (HEAD_DIM ** -0.5)).astype(jnp.bfloat16)
    keys = (stored_keys.astype(jnp.float32) * kv_scale[:, 0:1].astype(jnp.float32)).astype(jnp.bfloat16)
    values = (stored_values.astype(jnp.float32) * kv_scale[:, 1:2].astype(jnp.float32)).astype(jnp.bfloat16)
    groups = SEQUENCE_LENGTH // WINDOW
    q_all = queries.reshape(groups, WINDOW, QUERY_HEADS, HEAD_DIM)
    k_all = keys.reshape(groups, WINDOW, HEAD_DIM)
    v_all = values.reshape(groups, WINDOW, HEAD_DIM)
    s_all = doc_start.reshape(groups, WINDOW)

    def per_group(pieces):
        return attend_group(pieces[0], pieces[1], pieces[2], pieces[3])

    out = lax.map(per_group, (q_all, k_all, v_all, s_all))
    return out.reshape(SEQUENCE_LENGTH, QUERY_HEADS * HEAD_DIM)
```

```python
import math

import jax
import jax.numpy as jnp
from jax import lax
from jax.sharding import PartitionSpec as P

HEAD_DIM = 128
QUERY_HEADS = 3
Z_RING = 16
FAR = 1 << 24


def make_attend(q_set, pos_set, doc_set):

    def attend(carry, pieces):
        keys, values, key_pos = pieces
        count = keys.shape[0]
        block = math.gcd(count, 512)

        def step(state, number):
            key_block = lax.dynamic_slice_in_dim(keys, number * block, block, 0)
            value_block = lax.dynamic_slice_in_dim(values, number * block, block, 0)
            columns = lax.dynamic_slice_in_dim(key_pos, number * block, block, 0)
            allowed = (columns[None, :] >= doc_set[:, None]) & (
                columns[None, :] <= pos_set[:, None]
            )
            scores = jnp.einsum("hqd,kd->hqk", q_set, key_block, preferred_element_type=jnp.float32)
            scores = jnp.where(allowed[None], scores, -1e30)
            top_old, total_old, accum = state
            top_new = jnp.maximum(top_old, jnp.max(scores, axis=2))
            weights = jnp.where(allowed[None], jnp.exp(scores - top_new[..., None]), 0.0)
            fade = jnp.exp(top_old - top_new)
            total_new = total_old * fade + jnp.sum(weights, axis=2)
            accum = accum * fade[..., None] + jnp.einsum(
                "hqk,kd->hqd",
                weights.astype(jnp.bfloat16),
                value_block,
                preferred_element_type=jnp.float32,
            )
            return ((top_new, total_new, accum), None)

        state, _ = lax.scan(step, carry, jnp.arange(count // block))
        return state

    return attend


def gather_window(kv, n_ctx):
    z_ring = Z_RING if n_ctx % Z_RING == 0 else n_ctx
    rows = n_ctx // z_ring
    me = lax.axis_index("ctx")
    row, col = me // z_ring, me % z_ring
    stack = [kv]
    for k in range(1, rows):
        perm = [(c, c + k * z_ring) for c in range(n_ctx - k * z_ring)]
        stack.append(lax.ppermute(kv, "ctx", perm))
    stack = jnp.stack(stack)
    sources = [(0, 0)]
    got = [stack]
    fwd, bwd = stack, stack
    half = z_ring // 2
    for t in range(1, half + 1):
        fwd = lax.ppermute(
            fwd, "ctx", [(c, (c // z_ring) * z_ring + (c % z_ring + 1) % z_ring) for c in range(n_ctx)]
        )
        got.append(fwd)
        sources.append((t, -1))
        if t < z_ring - half:
            bwd = lax.ppermute(
                bwd, "ctx", [(c, (c // z_ring) * z_ring + (c % z_ring - 1) % z_ring) for c in range(n_ctx)]
            )
            got.append(bwd)
            sources.append((t, 1))
    blocks = jnp.stack(got)
    shift = jnp.array([t * d for t, d in sources], jnp.int32)
    src_col = (col + shift) % z_ring
    src_row = row - jnp.arange(rows, dtype=jnp.int32)
    src = src_row[None, :] * z_ring + src_col[:, None]
    valid = src_row[None, :] >= 0
    tokens = kv.shape[0]
    key_pos = src[:, :, None] * tokens + jnp.arange(tokens, dtype=jnp.int32)
    key_pos = jnp.where(valid[:, :, None], key_pos, FAR)
    return blocks.reshape(-1, kv.shape[1]), key_pos.reshape(-1)


def gather_weight(query_weight, n_ctx):
    spread = jnp.broadcast_to(query_weight[None], (n_ctx,) + query_weight.shape)
    rows = lax.all_to_all(spread, "ctx", 0, 0, tiled=False)
    rows = rows.reshape(-1, query_weight.shape[1])
    return lax.all_gather(rows, "stretch", axis=1, tiled=True)


def shards(hidden_in, query_weight, stored_keys, stored_values, kv_scale, doc_start, n_ctx):
    rows = hidden_in.shape[0]
    keys = (stored_keys.astype(jnp.float32) * kv_scale[:, 0:1].astype(jnp.float32)).astype(jnp.bfloat16)
    values = (stored_values.astype(jnp.float32) * kv_scale[:, 1:2].astype(jnp.float32)).astype(
        jnp.bfloat16
    )
    kv_all, key_pos = gather_window(jnp.concatenate([keys, values], axis=1), n_ctx)
    weight = gather_weight(query_weight, n_ctx)
    projected = jnp.dot(hidden_in, weight, preferred_element_type=jnp.float32)
    queries = (projected * HEAD_DIM ** (-0.5)).astype(jnp.bfloat16)
    queries = jnp.transpose(queries.reshape(rows, QUERY_HEADS, HEAD_DIM), (1, 0, 2))
    position = lax.axis_index("ctx") * rows + jnp.arange(rows, dtype=jnp.int32)
    attend = make_attend(queries, position, doc_start)
    initial = (
        jnp.full((QUERY_HEADS, rows), -1e30, jnp.float32),
        jnp.zeros((QUERY_HEADS, rows), jnp.float32),
        jnp.zeros((QUERY_HEADS, rows, HEAD_DIM), jnp.float32),
    )
    width = stored_keys.shape[1]
    top_final, total_final, accum_final = attend(
        initial, (kv_all[:, :width], kv_all[:, width:], key_pos)
    )
    mixed = (accum_final / total_final[..., None]).astype(jnp.bfloat16)
    flat = jnp.transpose(mixed, (1, 0, 2)).reshape(rows, QUERY_HEADS * HEAD_DIM)
    return flat


def solution(mesh):
    n_ctx = mesh.shape["ctx"]

    def body(*args):
        return shards(*args, n_ctx=n_ctx)

    return jax.shard_map(
        body,
        mesh=mesh,
        in_specs=(
            P(("stretch", "ctx"), None),
            P("ctx", "stretch"),
            P(("stretch", "ctx"), None),
            P(("stretch", "ctx"), None),
            P(("stretch", "ctx"), None),
            P(("stretch", "ctx")),
        ),
        out_specs=P(("stretch", "ctx"), None),
        check_vma=False,
    )
```

```python
import math

import jax
import jax.numpy as jnp
from jax import lax
from jax.sharding import PartitionSpec as P

HEAD_DIM = 128
QUERY_HEADS = 3
Z_RING = 16
FAR = 1 << 24


def make_attend(q_set, pos_set, doc_set):

    def attend(carry, pieces):
        keys, values, key_pos = pieces
        count = keys.shape[0]
        block = count

        def step(state, number):
            key_block = lax.dynamic_slice_in_dim(keys, number * block, block, 0)
            value_block = lax.dynamic_slice_in_dim(values, number * block, block, 0)
            columns = lax.dynamic_slice_in_dim(key_pos, number * block, block, 0)
            allowed = (columns[None, :] >= doc_set[:, None]) & (
                columns[None, :] <= pos_set[:, None]
            )
            scores = jnp.einsum("hqd,kd->hqk", q_set, key_block, preferred_element_type=jnp.float32)
            scores = jnp.where(allowed[None], scores, -1e30)
            top_old, total_old, accum = state
            top_new = jnp.maximum(top_old, jnp.max(scores, axis=2))
            weights = jnp.where(allowed[None], jnp.exp(scores - top_new[..., None]), 0.0)
            fade = jnp.exp(top_old - top_new)
            total_new = total_old * fade + jnp.sum(weights, axis=2)
            accum = accum * fade[..., None] + jnp.einsum(
                "hqk,kd->hqd",
                weights.astype(jnp.bfloat16),
                value_block,
                preferred_element_type=jnp.float32,
            )
            return ((top_new, total_new, accum), None)

        state, _ = lax.scan(step, carry, jnp.arange(count // block))
        return state

    return attend


def gather_window(kv, n_ctx):
    z_ring = Z_RING if n_ctx % Z_RING == 0 else n_ctx
    rows = n_ctx // z_ring
    me = lax.axis_index("ctx")
    row, col = me // z_ring, me % z_ring
    stack = [kv]
    for k in range(1, rows):
        perm = [(c, c + k * z_ring) for c in range(n_ctx - k * z_ring)]
        stack.append(lax.ppermute(kv, "ctx", perm))
    stack = jnp.stack(stack)
    sources = [(0, 0)]
    got = [stack]
    fwd, bwd = stack, stack
    half = z_ring // 2
    for t in range(1, half + 1):
        fwd = lax.ppermute(
            fwd, "ctx", [(c, (c // z_ring) * z_ring + (c % z_ring + 1) % z_ring) for c in range(n_ctx)]
        )
        got.append(fwd)
        sources.append((t, -1))
        if t < z_ring - half:
            bwd = lax.ppermute(
                bwd, "ctx", [(c, (c // z_ring) * z_ring + (c % z_ring - 1) % z_ring) for c in range(n_ctx)]
            )
            got.append(bwd)
            sources.append((t, 1))
    blocks = jnp.stack(got)
    shift = jnp.array([t * d for t, d in sources], jnp.int32)
    src_col = (col + shift) % z_ring
    src_row = row - jnp.arange(rows, dtype=jnp.int32)
    src = src_row[None, :] * z_ring + src_col[:, None]
    valid = src_row[None, :] >= 0
    tokens = kv.shape[0]
    key_pos = src[:, :, None] * tokens + jnp.arange(tokens, dtype=jnp.int32)
    key_pos = jnp.where(valid[:, :, None], key_pos, FAR)
    return blocks.reshape(-1, kv.shape[1]), key_pos.reshape(-1)


def gather_weight(query_weight, n_ctx):
    spread = jnp.broadcast_to(query_weight[None], (n_ctx,) + query_weight.shape)
    rows = lax.all_to_all(spread, "ctx", 0, 0, tiled=False)
    rows = rows.reshape(-1, query_weight.shape[1])
    return lax.all_gather(rows, "stretch", axis=1, tiled=True)


def shards(hidden_in, query_weight, stored_keys, stored_values, kv_scale, doc_start, n_ctx):
    rows = hidden_in.shape[0]
    keys = (stored_keys.astype(jnp.float32) * kv_scale[:, 0:1].astype(jnp.float32)).astype(jnp.bfloat16)
    values = (stored_values.astype(jnp.float32) * kv_scale[:, 1:2].astype(jnp.float32)).astype(
        jnp.bfloat16
    )
    kv_all, key_pos = gather_window(jnp.concatenate([keys, values], axis=1), n_ctx)
    weight = gather_weight(query_weight, n_ctx)
    projected = jnp.dot(hidden_in, weight, preferred_element_type=jnp.float32)
    queries = (projected * HEAD_DIM ** (-0.5)).astype(jnp.bfloat16)
    queries = jnp.transpose(queries.reshape(rows, QUERY_HEADS, HEAD_DIM), (1, 0, 2))
    position = lax.axis_index("ctx") * rows + jnp.arange(rows, dtype=jnp.int32)
    attend = make_attend(queries, position, doc_start)
    initial = (
        jnp.full((QUERY_HEADS, rows), -1e30, jnp.float32),
        jnp.zeros((QUERY_HEADS, rows), jnp.float32),
        jnp.zeros((QUERY_HEADS, rows, HEAD_DIM), jnp.float32),
    )
    width = stored_keys.shape[1]
    top_final, total_final, accum_final = attend(
        initial, (kv_all[:, :width], kv_all[:, width:], key_pos)
    )
    mixed = (accum_final / total_final[..., None]).astype(jnp.bfloat16)
    flat = jnp.transpose(mixed, (1, 0, 2)).reshape(rows, QUERY_HEADS * HEAD_DIM)
    return flat


def solution(mesh):
    n_ctx = mesh.shape["ctx"]

    def body(*args):
        return shards(*args, n_ctx=n_ctx)

    return jax.shard_map(
        body,
        mesh=mesh,
        in_specs=(
            P(("stretch", "ctx"), None),
            P("ctx", "stretch"),
            P(("stretch", "ctx"), None),
            P(("stretch", "ctx"), None),
            P(("stretch", "ctx"), None),
            P(("stretch", "ctx")),
        ),
        out_specs=P(("stretch", "ctx"), None),
        check_vma=False,
    )
```

```python
import math

import jax
import jax.numpy as jnp
from jax import lax
from jax.experimental import pallas as pl
from jax.experimental.pallas import tpu as pltpu
from jax.sharding import PartitionSpec as P

CHUNK = 512

def attn_kernel(q_ref, k_ref, v_ref, kp_ref, lo_ref, hi_ref, o_ref, s_ref):
    n = k_ref.shape[0] // CHUNK
    q = q_ref[...]
    lo = lo_ref[...]
    hi = hi_ref[...]

    def first(c, top):
        at = pl.multiple_of(c * CHUNK, CHUNK)
        s = lax.dot_general(q, k_ref[pl.ds(at, CHUNK), :], (((1,), (1,)), ((), ())),
                            preferred_element_type=jnp.float32)
        kp = kp_ref[:, pl.ds(at, CHUNK)]
        s = jnp.where((kp >= lo) & (kp <= hi), s, -1e30)
        s_ref[:, pl.ds(at, CHUNK)] = s
        return jnp.maximum(top, jnp.max(s, axis=1, keepdims=True))

    top = lax.fori_loop(0, n, first, jnp.full((q.shape[0], 1), -1e30, jnp.float32))

    def second(c, carry):
        total, accum = carry
        at = pl.multiple_of(c * CHUNK, CHUNK)
        s = s_ref[:, pl.ds(at, CHUNK)]
        kp = kp_ref[:, pl.ds(at, CHUNK)]
        w = jnp.where((kp >= lo) & (kp <= hi), jnp.exp(s - top), 0.0)
        total = total + jnp.sum(w, axis=1, keepdims=True)
        accum = accum + jnp.dot(w.astype(jnp.bfloat16), v_ref[pl.ds(at, CHUNK), :],
                                preferred_element_type=jnp.float32)
        return total, accum

    total, accum = lax.fori_loop(
        0, n, second,
        (jnp.zeros((q.shape[0], 1), jnp.float32), jnp.zeros((q.shape[0], v_ref.shape[1]), jnp.float32)))
    o_ref[...] = (accum / total).astype(o_ref.dtype)


def attend_pallas(q, keys, values, key_pos, lo, hi, interpret=False):
    rows = q.shape[0]
    return pl.pallas_call(
        attn_kernel,
        out_shape=jax.ShapeDtypeStruct((rows, values.shape[1]), jnp.bfloat16),
        scratch_shapes=[pltpu.VMEM((rows, keys.shape[0]), jnp.float32)],
        interpret=interpret,
    )(q, keys, values, key_pos.reshape(1, -1), lo.reshape(-1, 1), hi.reshape(-1, 1))


HEAD_DIM = 128
QUERY_HEADS = 3
Z_RING = 16
FAR = 1 << 24


def make_attend(q_set, pos_set, doc_set):

    def attend(carry, pieces):
        keys, values, key_pos = pieces
        count = keys.shape[0]
        block = count

        def step(state, number):
            key_block = lax.dynamic_slice_in_dim(keys, number * block, block, 0)
            value_block = lax.dynamic_slice_in_dim(values, number * block, block, 0)
            columns = lax.dynamic_slice_in_dim(key_pos, number * block, block, 0)
            allowed = (columns[None, :] >= doc_set[:, None]) & (
                columns[None, :] <= pos_set[:, None]
            )
            scores = jnp.einsum("hqd,kd->hqk", q_set, key_block, preferred_element_type=jnp.float32)
            scores = jnp.where(allowed[None], scores, -1e30)
            top_old, total_old, accum = state
            top_new = jnp.maximum(top_old, jnp.max(scores, axis=2))
            weights = jnp.where(allowed[None], jnp.exp(scores - top_new[..., None]), 0.0)
            fade = jnp.exp(top_old - top_new)
            total_new = total_old * fade + jnp.sum(weights, axis=2)
            accum = accum * fade[..., None] + jnp.einsum(
                "hqk,kd->hqd",
                weights.astype(jnp.bfloat16),
                value_block,
                preferred_element_type=jnp.float32,
            )
            return ((top_new, total_new, accum), None)

        state, _ = lax.scan(step, carry, jnp.arange(count // block))
        return state

    return attend


def gather_window(kv, n_ctx):
    z_ring = Z_RING if n_ctx % Z_RING == 0 else n_ctx
    rows = n_ctx // z_ring
    me = lax.axis_index("ctx")
    row, col = me // z_ring, me % z_ring
    stack = [kv]
    for k in range(1, rows):
        perm = [(c, c + k * z_ring) for c in range(n_ctx - k * z_ring)]
        stack.append(lax.ppermute(kv, "ctx", perm))
    stack = jnp.stack(stack)
    sources = [(0, 0)]
    got = [stack]
    fwd, bwd = stack, stack
    half = z_ring // 2
    for t in range(1, half + 1):
        fwd = lax.ppermute(
            fwd, "ctx", [(c, (c // z_ring) * z_ring + (c % z_ring + 1) % z_ring) for c in range(n_ctx)]
        )
        got.append(fwd)
        sources.append((t, -1))
        if t < z_ring - half:
            bwd = lax.ppermute(
                bwd, "ctx", [(c, (c // z_ring) * z_ring + (c % z_ring - 1) % z_ring) for c in range(n_ctx)]
            )
            got.append(bwd)
            sources.append((t, 1))
    blocks = jnp.stack(got)
    shift = jnp.array([t * d for t, d in sources], jnp.int32)
    src_col = (col + shift) % z_ring
    src_row = row - jnp.arange(rows, dtype=jnp.int32)
    src = src_row[None, :] * z_ring + src_col[:, None]
    valid = src_row[None, :] >= 0
    tokens = kv.shape[0]
    key_pos = src[:, :, None] * tokens + jnp.arange(tokens, dtype=jnp.int32)
    key_pos = jnp.where(valid[:, :, None], key_pos, FAR)
    return blocks.reshape(-1, kv.shape[1]), key_pos.reshape(-1)


def gather_weight(query_weight, n_ctx):
    spread = jnp.broadcast_to(query_weight[None], (n_ctx,) + query_weight.shape)
    rows = lax.all_to_all(spread, "ctx", 0, 0, tiled=False)
    rows = rows.reshape(-1, query_weight.shape[1])
    return lax.all_gather(rows, "stretch", axis=1, tiled=True)


def shards(hidden_in, query_weight, stored_keys, stored_values, kv_scale, doc_start, n_ctx):
    rows = hidden_in.shape[0]
    keys = (stored_keys.astype(jnp.float32) * kv_scale[:, 0:1].astype(jnp.float32)).astype(jnp.bfloat16)
    values = (stored_values.astype(jnp.float32) * kv_scale[:, 1:2].astype(jnp.float32)).astype(
        jnp.bfloat16
    )
    kv_all, key_pos = gather_window(jnp.concatenate([keys, values], axis=1), n_ctx)
    weight = gather_weight(query_weight, n_ctx)
    projected = jnp.dot(hidden_in, weight, preferred_element_type=jnp.float32)
    queries = (projected * HEAD_DIM ** (-0.5)).astype(jnp.bfloat16)
    queries = jnp.transpose(queries.reshape(rows, QUERY_HEADS, HEAD_DIM), (1, 0, 2))
    position = lax.axis_index("ctx") * rows + jnp.arange(rows, dtype=jnp.int32)
    width = stored_keys.shape[1]
    mixed = attend_pallas(
        queries.reshape(QUERY_HEADS * rows, HEAD_DIM),
        kv_all[:, :width],
        kv_all[:, width:],
        key_pos,
        jnp.tile(doc_start, QUERY_HEADS),
        jnp.tile(position, QUERY_HEADS),
    ).reshape(QUERY_HEADS, rows, HEAD_DIM)
    flat = jnp.transpose(mixed, (1, 0, 2)).reshape(rows, QUERY_HEADS * HEAD_DIM)
    return flat


def solution(mesh):
    n_ctx = mesh.shape["ctx"]

    def body(*args):
        return shards(*args, n_ctx=n_ctx)

    return jax.shard_map(
        body,
        mesh=mesh,
        in_specs=(
            P(("stretch", "ctx"), None),
            P("ctx", "stretch"),
            P(("stretch", "ctx"), None),
            P(("stretch", "ctx"), None),
            P(("stretch", "ctx"), None),
            P(("stretch", "ctx")),
        ),
        out_specs=P(("stretch", "ctx"), None),
        check_vma=False,
    )
```

```python
import math

import jax
import jax.numpy as jnp
from jax import lax
from jax.experimental import pallas as pl
from jax.experimental.pallas import tpu as pltpu
from jax.sharding import PartitionSpec as P

CHUNK = 512

def attn_kernel(kmin_ref, kmax_ref, bound_ref, q_ref, k_ref, v_ref, kp_ref, lo_ref, hi_ref, o_ref, s_ref):
    n = k_ref.shape[0] // CHUNK
    q = q_ref[...]
    lo = lo_ref[...]
    hi = hi_ref[...]

    def live(c):
        return (kmin_ref[c] <= bound_ref[1]) & (kmax_ref[c] >= bound_ref[0])

    def first(c, top):
        return lax.cond(live(c), lambda: first_live(c, top), lambda: top)

    def first_live(c, top):
        at = pl.multiple_of(c * CHUNK, CHUNK)
        s = lax.dot_general(q, k_ref[pl.ds(at, CHUNK), :], (((1,), (1,)), ((), ())),
                            preferred_element_type=jnp.float32)
        kp = kp_ref[:, pl.ds(at, CHUNK)]
        s = jnp.where((kp >= lo) & (kp <= hi), s, -1e30)
        s_ref[:, pl.ds(at, CHUNK)] = s
        return jnp.maximum(top, jnp.max(s, axis=1, keepdims=True))

    top = lax.fori_loop(0, n, first, jnp.full((q.shape[0], 1), -1e30, jnp.float32))

    def second(c, carry):
        return lax.cond(live(c), lambda: second_live(c, carry), lambda: carry)

    def second_live(c, carry):
        total, accum = carry
        at = pl.multiple_of(c * CHUNK, CHUNK)
        s = s_ref[:, pl.ds(at, CHUNK)]
        kp = kp_ref[:, pl.ds(at, CHUNK)]
        w = jnp.where((kp >= lo) & (kp <= hi), jnp.exp(s - top), 0.0)
        total = total + jnp.sum(w, axis=1, keepdims=True)
        accum = accum + jnp.dot(w.astype(jnp.bfloat16), v_ref[pl.ds(at, CHUNK), :],
                                preferred_element_type=jnp.float32)
        return total, accum

    total, accum = lax.fori_loop(
        0, n, second,
        (jnp.zeros((q.shape[0], 1), jnp.float32), jnp.zeros((q.shape[0], v_ref.shape[1]), jnp.float32)))
    o_ref[...] = (accum / total).astype(o_ref.dtype)


def attend_pallas(q, keys, values, key_pos, lo, hi, interpret=False):
    rows = q.shape[0]
    chunks = key_pos.reshape(-1, CHUNK)
    kmin = jnp.min(chunks, axis=1)
    kmax = jnp.max(jnp.where(chunks < (1 << 23), chunks, -1), axis=1)
    bound = jnp.stack([jnp.min(lo), jnp.max(hi)])
    smem = pl.BlockSpec(memory_space=pltpu.SMEM)
    vmem = pl.BlockSpec(memory_space=pltpu.VMEM)
    return pl.pallas_call(
        attn_kernel,
        out_shape=jax.ShapeDtypeStruct((rows, values.shape[1]), jnp.bfloat16),
        scratch_shapes=[pltpu.VMEM((rows, keys.shape[0]), jnp.float32)],
        in_specs=[smem, smem, smem, vmem, vmem, vmem, vmem, vmem, vmem],
        out_specs=vmem,
        interpret=interpret,
    )(kmin, kmax, bound, q, keys, values, key_pos.reshape(1, -1), lo.reshape(-1, 1), hi.reshape(-1, 1))


HEAD_DIM = 128
QUERY_HEADS = 3
Z_RING = 16
FAR = 1 << 24


def make_attend(q_set, pos_set, doc_set):

    def attend(carry, pieces):
        keys, values, key_pos = pieces
        count = keys.shape[0]
        block = count

        def step(state, number):
            key_block = lax.dynamic_slice_in_dim(keys, number * block, block, 0)
            value_block = lax.dynamic_slice_in_dim(values, number * block, block, 0)
            columns = lax.dynamic_slice_in_dim(key_pos, number * block, block, 0)
            allowed = (columns[None, :] >= doc_set[:, None]) & (
                columns[None, :] <= pos_set[:, None]
            )
            scores = jnp.einsum("hqd,kd->hqk", q_set, key_block, preferred_element_type=jnp.float32)
            scores = jnp.where(allowed[None], scores, -1e30)
            top_old, total_old, accum = state
            top_new = jnp.maximum(top_old, jnp.max(scores, axis=2))
            weights = jnp.where(allowed[None], jnp.exp(scores - top_new[..., None]), 0.0)
            fade = jnp.exp(top_old - top_new)
            total_new = total_old * fade + jnp.sum(weights, axis=2)
            accum = accum * fade[..., None] + jnp.einsum(
                "hqk,kd->hqd",
                weights.astype(jnp.bfloat16),
                value_block,
                preferred_element_type=jnp.float32,
            )
            return ((top_new, total_new, accum), None)

        state, _ = lax.scan(step, carry, jnp.arange(count // block))
        return state

    return attend


def gather_window(kv, n_ctx):
    z_ring = Z_RING if n_ctx % Z_RING == 0 else n_ctx
    rows = n_ctx // z_ring
    me = lax.axis_index("ctx")
    row, col = me // z_ring, me % z_ring
    stack = [kv]
    for k in range(1, rows):
        perm = [(c, c + k * z_ring) for c in range(n_ctx - k * z_ring)]
        stack.append(lax.ppermute(kv, "ctx", perm))
    stack = jnp.stack(stack)
    sources = [(0, 0)]
    got = [stack]
    fwd, bwd = stack, stack
    half = z_ring // 2
    for t in range(1, half + 1):
        fwd = lax.ppermute(
            fwd, "ctx", [(c, (c // z_ring) * z_ring + (c % z_ring + 1) % z_ring) for c in range(n_ctx)]
        )
        got.append(fwd)
        sources.append((t, -1))
        if t < z_ring - half:
            bwd = lax.ppermute(
                bwd, "ctx", [(c, (c // z_ring) * z_ring + (c % z_ring - 1) % z_ring) for c in range(n_ctx)]
            )
            got.append(bwd)
            sources.append((t, 1))
    blocks = jnp.stack(got)
    shift = jnp.array([t * d for t, d in sources], jnp.int32)
    src_col = (col + shift) % z_ring
    src_row = row - jnp.arange(rows, dtype=jnp.int32)
    src = src_row[None, :] * z_ring + src_col[:, None]
    valid = src_row[None, :] >= 0
    tokens = kv.shape[0]
    key_pos = src[:, :, None] * tokens + jnp.arange(tokens, dtype=jnp.int32)
    key_pos = jnp.where(valid[:, :, None], key_pos, FAR)
    return blocks.reshape(-1, kv.shape[1]), key_pos.reshape(-1)


def gather_weight(query_weight, n_ctx):
    spread = jnp.broadcast_to(query_weight[None], (n_ctx,) + query_weight.shape)
    rows = lax.all_to_all(spread, "ctx", 0, 0, tiled=False)
    rows = rows.reshape(-1, query_weight.shape[1])
    return lax.all_gather(rows, "stretch", axis=1, tiled=True)


def shards(hidden_in, query_weight, stored_keys, stored_values, kv_scale, doc_start, n_ctx):
    rows = hidden_in.shape[0]
    keys = (stored_keys.astype(jnp.float32) * kv_scale[:, 0:1].astype(jnp.float32)).astype(jnp.bfloat16)
    values = (stored_values.astype(jnp.float32) * kv_scale[:, 1:2].astype(jnp.float32)).astype(
        jnp.bfloat16
    )
    kv_all, key_pos = gather_window(jnp.concatenate([keys, values], axis=1), n_ctx)
    weight = gather_weight(query_weight, n_ctx)
    projected = jnp.dot(hidden_in, weight, preferred_element_type=jnp.float32)
    queries = (projected * HEAD_DIM ** (-0.5)).astype(jnp.bfloat16)
    queries = jnp.transpose(queries.reshape(rows, QUERY_HEADS, HEAD_DIM), (1, 0, 2))
    position = lax.axis_index("ctx") * rows + jnp.arange(rows, dtype=jnp.int32)
    width = stored_keys.shape[1]
    mixed = attend_pallas(
        queries.reshape(QUERY_HEADS * rows, HEAD_DIM),
        kv_all[:, :width],
        kv_all[:, width:],
        key_pos,
        jnp.tile(doc_start, QUERY_HEADS),
        jnp.tile(position, QUERY_HEADS),
    ).reshape(QUERY_HEADS, rows, HEAD_DIM)
    flat = jnp.transpose(mixed, (1, 0, 2)).reshape(rows, QUERY_HEADS * HEAD_DIM)
    return flat


def solution(mesh):
    n_ctx = mesh.shape["ctx"]

    def body(*args):
        return shards(*args, n_ctx=n_ctx)

    return jax.shard_map(
        body,
        mesh=mesh,
        in_specs=(
            P(("stretch", "ctx"), None),
            P("ctx", "stretch"),
            P(("stretch", "ctx"), None),
            P(("stretch", "ctx"), None),
            P(("stretch", "ctx"), None),
            P(("stretch", "ctx")),
        ),
        out_specs=P(("stretch", "ctx"), None),
        check_vma=False,
    )
```
